256 devices in a mesh: dp: 16 (over y_lo, x, core), tensor: 16 (over z, y_hi).
Axes of the slice: x: 4, y: 4 (y_hi: 2, y_lo: 2; y = y_hi * 2 + y_lo), z: 8, core: 2. Of those that a mesh axis runs over, the one named last changes fastest.
Arguments:
- gate_pre: bfloat16 [8192, 14336], P('dp', 'tensor'), may hold values from -6 to 6
- up_pre: bfloat16 [8192, 14336], P('dp', 'tensor'), may hold values from -6 to 6
- grad_out: bfloat16 [8192, 4096], P(('dp', 'tensor')), may hold values from -24 to 24
- codes: bfloat16 [14336, 4096], P('tensor'), as said below
- scales: int32 [448, 4096], P('tensor'), may hold values from 117 to 120
Outputs:
- out: bfloat16 [8192, 4096], P(('dp', 'tensor'))
- grad_gate: bfloat16 [8192, 14336], P('dp', 'tensor')
- grad_up: bfloat16 [8192, 14336], P('dp', 'tensor')
- grad_weight: bfloat16 [14336, 4096], P('tensor', 'dp')
The draws below stay inside these ranges and needn't reach their ends.
Inputs may be any that keep to these rules, and one draw needn't show every extreme that they name: `codes`: every entry is an FP8 E4M3 normal value (sign, exponent field 4 to 9, three mantissa bits), held exactly.
All inputs are finite; a program needn't handle non-finite values.
Results may differ from the reference program's by a relative error of at most 0.022.
Values may be sent and summed in bfloat16 or wider, within the bound.
No kernel may reach another device: no remote copies, remote signals or barrier semaphores. Data moves between devices by JAX's collectives and lax.ppermute only.
A program may use at most 128 MiB of HBM per device.

```python
import jax
import jax.numpy as jnp
from jax import lax

D = 4096
FF = 14336
TOK_DEV = 512
TOKENS = 8192
N_DP = 16
N_TENSOR = 16


def draw_codes(key, part):
    key_sign, key_expo, key_mant = jax.random.split(key, 3)
    sign_bits = jax.random.randint(key_sign, (FF, D), 0, 2)
    exponent = jax.random.randint(key_expo, (FF, D), 4, 10)
    mantissa = jax.random.randint(key_mant, (FF, D), 0, 8)
    value = (1.0 - 2.0 * sign_bits.astype(jnp.float32)) * (1.0 + mantissa.astype(jnp.float32) / 8.0) * jnp.exp2(exponent.astype(jnp.float32) - 7.0)
    return value.astype(jnp.bfloat16)


def with_ends(entries, key, smallest, high):
    place = [jax.random.randint(jax.random.fold_in(key, axis), (), 0, length) for axis, length in enumerate(entries.shape)]
    longest = entries.shape.index(max(entries.shape))
    next_to = place[:longest] + [(place[longest] + 1) % entries.shape[longest]] + place[longest + 1:]
    return entries.at[tuple(place)].set(smallest).at[tuple(next_to)].set(high)


def strengthened(values, stream_key, source, target, blocks, factor):
    owner, partner = [(jnp.arange(values.shape[dim]) // (values.shape[dim] // blocks)).reshape([-1 if axis == dim else 1 for axis in range(values.ndim)]) for dim in (source, target)]
    chosen = jax.random.permutation(stream_key, blocks)[partner]
    strong = (owner == chosen) | (owner == (partner + blocks // 2) % blocks)
    return jnp.where(strong, factor * values, values)


def block_scale(rng, extent, shards, least, largest):
    gain, own = 1.0, jax.random.fold_in(rng, 6)
    for dim, blocks in shards:
        heights = jnp.exp(jax.random.uniform(jax.random.fold_in(own, dim), (blocks,), jnp.float32, least / len(shards), largest / len(shards)))
        gain = gain * jnp.repeat(heights, extent[dim] // blocks).reshape([-1 if axis == dim else 1 for axis in range(len(extent))])
    return gain


def bell_draw(rng, extent, deviation, limit, pieces=(), kind=jnp.bfloat16):
    factor_of = block_scale(rng, extent, pieces, -0.22, 0.18) if pieces else 1.0
    drawn = jax.random.normal(rng, extent, jnp.float32) * deviation * factor_of
    return jnp.minimum(jnp.maximum(drawn, -limit), limit).astype(kind)


def gaussian_with(own_key, extent, deviation, bound, cuts, heavy, held_as=jnp.bfloat16):
    entries = deviation * jax.random.normal(own_key, extent, jnp.float32)
    if cuts:
        entries = entries * block_scale(own_key, extent, cuts, -0.22, 0.18)
    return jnp.clip(strengthened(entries, jax.random.fold_in(own_key, 3), *heavy), -bound, bound).astype(held_as)


def setup_inputs(seed: int = 0) -> dict:
    arg_keys = jax.random.split(jax.random.key(seed), 6)
    gate_pre = bell_draw(arg_keys[0], (TOKENS, FF), 1.0, 6.0, ((0, 16), (1, 16)))
    up_pre = bell_draw(arg_keys[1], (TOKENS, FF), 1.0, 6.0, ((0, 16), (1, 16)))
    grad_out = gaussian_with(arg_keys[2], (TOKENS, D), 1.0, 24.0, ((0, 256),), (0, 1, 256, 6.0))
    codes = draw_codes(jax.random.fold_in(arg_keys[5], 71), 0)
    scales = with_ends(jax.random.randint(arg_keys[4], (FF // 32, D), 117, 121), jax.random.fold_in(arg_keys[4], 1), 117, 120).astype(jnp.int32)
    return {"gate_pre": gate_pre, "up_pre": up_pre, "grad_out": grad_out, "codes": codes, "scales": scales}


def decode(codes, scales):
    factor = jnp.exp2(scales.astype(jnp.float32) - 127.0).astype(jnp.bfloat16)
    blocks = codes.reshape(FF // 32, 32, D) * factor[:, None, :]
    return blocks.reshape(FF, D)


def reference(gate_pre, up_pre, grad_out, codes, scales):
    weight = decode(codes, scales)
    gate_value = gate_pre.astype(jnp.float32)
    up_value = up_pre.astype(jnp.float32)
    sigmoid_gate = jax.nn.sigmoid(gate_value)
    hidden = (gate_value * sigmoid_gate * up_value).astype(jnp.bfloat16)
    width = FF // N_TENSOR

    def add_block(index, total):
        start = (index * width).astype(jnp.int32)
        hidden_block = lax.dynamic_slice_in_dim(hidden, start, width, 1)
        weight_block = lax.dynamic_slice_in_dim(weight, start, width, 0)
        partial_sum = jnp.dot(hidden_block, weight_block, preferred_element_type=jnp.float32).astype(jnp.bfloat16)
        return total + lax.optimization_barrier(partial_sum).astype(jnp.float32)

    out = lax.fori_loop(0, N_TENSOR, add_block, jnp.zeros((TOKENS, D), jnp.float32)).astype(jnp.bfloat16)
    grad_hidden = jnp.dot(grad_out, weight.T, preferred_element_type=jnp.float32)
    grad_gate = (grad_hidden * up_value * sigmoid_gate * (1.0 + gate_value * (1.0 - sigmoid_gate))).astype(jnp.bfloat16)
    grad_up = (grad_hidden * gate_value * sigmoid_gate).astype(jnp.bfloat16)

    def add_replica(index, total):
        start = (index * TOK_DEV).astype(jnp.int32)
        hidden_rows = lax.dynamic_slice_in_dim(hidden, start, TOK_DEV, 0)
        grad_rows = lax.dynamic_slice_in_dim(grad_out, start, TOK_DEV, 0)
        partial_sum = jnp.dot(hidden_rows.T, grad_rows, preferred_element_type=jnp.float32).astype(jnp.bfloat16)
        return total + lax.optimization_barrier(partial_sum).astype(jnp.float32)

    grad_weight = lax.fori_loop(0, N_DP, add_replica, jnp.zeros((FF, D), jnp.float32)).astype(jnp.bfloat16)
    return (out, grad_gate, grad_up, grad_weight)
```

```python
import jax
import jax.numpy as jnp
from jax import lax
from jax.sharding import Mesh, PartitionSpec as P

DP = ("dy", "dx", "dc")
TP = ("tz", "ty")


def decode(codes, scales):
    factor = jnp.exp2(scales.astype(jnp.float32) - 127.0).astype(jnp.bfloat16)
    blocks = codes.reshape(scales.shape[0], 32, codes.shape[1]) * factor[:, None, :]
    return blocks.reshape(codes.shape)


def weight_gradient(hidden, cotangent):
    partial_grad = lax.dot_general(
        hidden, cotangent, (((0,), (0,)), ((), ())), preferred_element_type=jnp.float32
    )
    return lax.psum_scatter(
        partial_grad.astype(jnp.bfloat16), DP, scatter_dimension=1, tiled=True
    )


def per_device(gate_pre, up_pre, grad_out, codes, scales):
    weight = decode(codes, scales)
    gate_value = gate_pre.astype(jnp.float32)
    up_value = up_pre.astype(jnp.float32)
    sigmoid_gate = jax.nn.sigmoid(gate_value)
    hidden = (gate_value * sigmoid_gate * up_value).astype(jnp.bfloat16)
    partial_out = jnp.dot(hidden, weight, preferred_element_type=jnp.float32).astype(jnp.bfloat16)
    out = lax.psum_scatter(partial_out, "tz", scatter_dimension=0, tiled=True)
    out = lax.psum_scatter(out, "ty", scatter_dimension=0, tiled=True)
    cotangent = lax.all_gather(grad_out, "ty", axis=0, tiled=True)
    cotangent = lax.all_gather(cotangent, "tz", axis=0, tiled=True)
    grad_hidden = lax.dot_general(
        cotangent, weight, (((1,), (1,)), ((), ())), preferred_element_type=jnp.float32
    )
    grad_weight = weight_gradient(hidden, cotangent)
    grad_gate = (
        grad_hidden * up_value * sigmoid_gate * (1.0 + gate_value * (1.0 - sigmoid_gate))
    ).astype(jnp.bfloat16)
    grad_up = (grad_hidden * gate_value * sigmoid_gate).astype(jnp.bfloat16)
    return (out, grad_gate, grad_up, grad_weight)


def split_mesh(mesh):
    n_dp, n_tensor = mesh.shape["dp"], mesh.shape["tensor"]
    devices = mesh.devices.reshape(2, n_dp // 4, 2, n_tensor // 2, 2)
    return Mesh(devices, DP + TP)


def solution(mesh):
    fine = split_mesh(mesh)
    in_specs = (
        P(DP, TP),
        P(DP, TP),
        P(DP + TP, None),
        P(TP, None),
        P(TP, None),
    )
    out_specs = (P(DP + TP, None), P(DP, TP), P(DP, TP), P(TP, DP))
    return jax.shard_map(
        per_device, mesh=fine, in_specs=in_specs, out_specs=out_specs, check_vma=False
    )
```

```python
import jax
import jax.numpy as jnp
from jax import lax
from jax.sharding import Mesh, PartitionSpec as P

DP = ("dy", "dx", "dc")
TP = ("tz", "ty")


def decode(codes, scales):
    factor = jnp.exp2(scales.astype(jnp.float32) - 127.0).astype(jnp.bfloat16)
    blocks = codes.reshape(scales.shape[0], 32, codes.shape[1]) * factor[:, None, :]
    return blocks.reshape(codes.shape)


def exchange(value, axis, size, shift):
    perm = [(i, (i + shift) % size) for i in range(size)]
    return lax.ppermute(value, axis, perm)


def weight_gradient(hidden, cotangent):
    partial_grad = lax.dot_general(
        hidden, cotangent, (((0,), (0,)), ((), ())), preferred_element_type=jnp.float32
    ).astype(jnp.bfloat16)
    rows = partial_grad.shape[0]
    n_x = partial_grad.shape[1] // 1024
    parts = partial_grad.reshape(rows, 2, n_x, 2, 256)
    dc = lax.axis_index("dc")
    mine = jnp.take(parts, dc, axis=3)
    theirs = jnp.take(parts, 1 - dc, axis=3)
    total = mine.astype(jnp.float32) + exchange(theirs, "dc", 2, 1).astype(jnp.float32)
    sent = total.astype(jnp.bfloat16)
    dx = lax.axis_index("dx")
    acc = jnp.take(total, dx, axis=2)
    for shift in range(1, n_x):
        block = jnp.take(sent, (dx + shift) % n_x, axis=2)
        acc = acc + exchange(block, "dx", n_x, shift).astype(jnp.float32)
    dy = lax.axis_index("dy")
    sent = acc.astype(jnp.bfloat16)
    acc = jnp.take(acc, dy, axis=1) + exchange(jnp.take(sent, 1 - dy, axis=1), "dy", 2, 1).astype(jnp.float32)
    return acc.astype(jnp.bfloat16)


def per_device(gate_pre, up_pre, grad_out, codes, scales):
    weight = decode(codes, scales)
    gate_value = gate_pre.astype(jnp.float32)
    up_value = up_pre.astype(jnp.float32)
    sigmoid_gate = jax.nn.sigmoid(gate_value)
    hidden = (gate_value * sigmoid_gate * up_value).astype(jnp.bfloat16)
    partial_out = jnp.dot(hidden, weight, preferred_element_type=jnp.float32).astype(jnp.bfloat16)
    out = lax.psum_scatter(partial_out, "tz", scatter_dimension=0, tiled=True)
    out = lax.psum_scatter(out, "ty", scatter_dimension=0, tiled=True)
    cotangent = lax.all_gather(grad_out, "ty", axis=0, tiled=True)
    cotangent = lax.all_gather(cotangent, "tz", axis=0, tiled=True)
    grad_hidden = lax.dot_general(
        cotangent, weight, (((1,), (1,)), ((), ())), preferred_element_type=jnp.float32
    )
    grad_weight = weight_gradient(hidden, cotangent)
    grad_gate = (
        grad_hidden * up_value * sigmoid_gate * (1.0 + gate_value * (1.0 - sigmoid_gate))
    ).astype(jnp.bfloat16)
    grad_up = (grad_hidden * gate_value * sigmoid_gate).astype(jnp.bfloat16)
    return (out, grad_gate, grad_up, grad_weight)


def split_mesh(mesh):
    n_dp, n_tensor = mesh.shape["dp"], mesh.shape["tensor"]
    devices = mesh.devices.reshape(2, n_dp // 4, 2, n_tensor // 2, 2)
    return Mesh(devices, DP + TP)


def solution(mesh):
    fine = split_mesh(mesh)
    in_specs = (
        P(DP, TP),
        P(DP, TP),
        P(DP + TP, None),
        P(TP, None),
        P(TP, None),
    )
    out_specs = (P(DP + TP, None), P(DP, TP), P(DP, TP), P(TP, DP))
    return jax.shard_map(
        per_device, mesh=fine, in_specs=in_specs, out_specs=out_specs, check_vma=False
    )
```

```python
import jax
import jax.numpy as jnp
from jax import lax
from jax.experimental.layout import Layout, with_layout_constraint
from jax.sharding import Mesh, PartitionSpec as P

DP = ("dy", "dx", "dc")
TP = ("tz", "ty")


def decode(codes, scales):
    factor = jnp.exp2(scales.astype(jnp.float32) - 127.0).astype(jnp.bfloat16)
    blocks = codes.reshape(scales.shape[0], 32, codes.shape[1]) * factor[:, None, :]
    return blocks.reshape(codes.shape)


def exchange(value, axis, size, shift):
    perm = [(i, (i + shift) % size) for i in range(size)]
    return lax.ppermute(value, axis, perm)


def weight_gradient(hidden, cotangent):
    n_x = cotangent.shape[1] // 1024
    width = 256
    partial = lax.dot_general(
        cotangent, hidden, (((0,), (0,)), ((), ())), preferred_element_type=jnp.float32
    ).astype(jnp.bfloat16)
    partial = with_layout_constraint(partial, Layout(major_to_minor=(0, 1)))
    parts = partial.reshape(2, n_x, 2, width, partial.shape[1])
    dc = lax.axis_index("dc")
    mine = jnp.take(parts, dc, axis=2)
    arrived = exchange(jnp.take(parts, 1 - dc, axis=2), "dc", 2, 1)
    total = mine.astype(jnp.float32) + arrived.astype(jnp.float32)
    total = with_layout_constraint(total, Layout(major_to_minor=(0, 1, 2, 3)))
    sent = total.astype(jnp.bfloat16)
    dx = lax.axis_index("dx")
    acc = jnp.take(total, dx, axis=1)
    for shift in range(1, n_x):
        block = jnp.take(sent, (dx + shift) % n_x, axis=1)
        acc = acc + exchange(block, "dx", n_x, shift).astype(jnp.float32)
    dy = lax.axis_index("dy")
    sent = acc.astype(jnp.bfloat16)
    acc = jnp.take(acc, dy, axis=0) + exchange(jnp.take(sent, 1 - dy, axis=0), "dy", 2, 1).astype(jnp.float32)
    acc = with_layout_constraint(acc.astype(jnp.bfloat16), Layout(major_to_minor=(0, 1)))
    return acc.T


def per_device(gate_pre, up_pre, grad_out, codes, scales):
    weight = decode(codes, scales)
    gate_value = gate_pre.astype(jnp.float32)
    up_value = up_pre.astype(jnp.float32)
    sigmoid_gate = jax.nn.sigmoid(gate_value)
    hidden = (gate_value * sigmoid_gate * up_value).astype(jnp.bfloat16)
    partial_out = jnp.dot(hidden, weight, preferred_element_type=jnp.float32).astype(jnp.bfloat16)
    out = lax.psum_scatter(partial_out, "tz", scatter_dimension=0, tiled=True)
    rows = out.shape[0] // 2
    ty = lax.axis_index("ty")
    out = lax.dynamic_slice_in_dim(out, ty * rows, rows, 0).astype(jnp.float32) + exchange(
        lax.dynamic_slice_in_dim(out, (1 - ty) * rows, rows, 0), "ty", 2, 1
    ).astype(jnp.float32)
    out = out.astype(jnp.bfloat16)
    cotangent = lax.all_gather(grad_out, "ty", axis=0, tiled=True)
    cotangent = lax.all_gather(cotangent, "tz", axis=0, tiled=True)
    grad_hidden = lax.dot_general(
        cotangent, weight, (((1,), (1,)), ((), ())), preferred_element_type=jnp.float32
    )
    grad_weight = weight_gradient(hidden, cotangent)
    grad_gate = (
        grad_hidden * up_value * sigmoid_gate * (1.0 + gate_value * (1.0 - sigmoid_gate))
    ).astype(jnp.bfloat16)
    grad_up = (grad_hidden * gate_value * sigmoid_gate).astype(jnp.bfloat16)
    return (out, grad_gate, grad_up, grad_weight)


def split_mesh(mesh):
    n_dp, n_tensor = mesh.shape["dp"], mesh.shape["tensor"]
    devices = mesh.devices.reshape(2, n_dp // 4, 2, n_tensor // 2, 2)
    return Mesh(devices, DP + TP)


def solution(mesh):
    fine = split_mesh(mesh)
    in_specs = (
        P(DP, TP),
        P(DP, TP),
        P(DP + TP, None),
        P(TP, None),
        P(TP, None),
    )
    out_specs = (P(DP + TP, None), P(DP, TP), P(DP, TP), P(TP, DP))
    return jax.shard_map(
        per_device, mesh=fine, in_specs=in_specs, out_specs=out_specs, check_vma=False
    )
```

```python
import jax
import jax.numpy as jnp
from jax import lax
from jax.experimental.layout import Layout, with_layout_constraint
from jax.sharding import Mesh, PartitionSpec as P

DP = ("dy", "dx", "dc")
TP = ("tz", "ty")


def decode(codes, scales):
    factor = jnp.exp2(scales.astype(jnp.float32) - 127.0).astype(jnp.bfloat16)
    blocks = codes.reshape(scales.shape[0], 32, codes.shape[1]) * factor[:, None, :]
    return blocks.reshape(codes.shape)


def exchange(value, axis, size, shift):
    perm = [(i, (i + shift) % size) for i in range(size)]
    return lax.ppermute(value, axis, perm)


def weight_gradient(hidden, cotangent):
    lanes = hidden.shape[1] // 128
    cut = 128 * (lanes // 2)
    return jnp.concatenate(
        [reduce_chunk(hidden[:, :cut], cotangent), reduce_chunk(hidden[:, cut:], cotangent)], axis=0
    )


def reduce_chunk(hidden, cotangent):
    n_x = cotangent.shape[1] // 1024
    width = 256
    partial = lax.dot_general(
        cotangent, hidden, (((0,), (0,)), ((), ())), preferred_element_type=jnp.float32
    ).astype(jnp.bfloat16)
    partial = with_layout_constraint(partial, Layout(major_to_minor=(0, 1)))
    parts = partial.reshape(2, n_x, 2, width, partial.shape[1])
    dc = lax.axis_index("dc")
    mine = jnp.take(parts, dc, axis=2)
    arrived = exchange(jnp.take(parts, 1 - dc, axis=2), "dc", 2, 1)
    total = mine.astype(jnp.float32) + arrived.astype(jnp.float32)
    total = with_layout_constraint(total, Layout(major_to_minor=(0, 1, 2, 3)))
    sent = total.astype(jnp.bfloat16)
    dx = lax.axis_index("dx")
    acc = jnp.take(total, dx, axis=1)
    for shift in range(1, n_x):
        block = jnp.take(sent, (dx + shift) % n_x, axis=1)
        acc = acc + exchange(block, "dx", n_x, shift).astype(jnp.float32)
    dy = lax.axis_index("dy")
    sent = acc.astype(jnp.bfloat16)
    acc = jnp.take(acc, dy, axis=0) + exchange(jnp.take(sent, 1 - dy, axis=0), "dy", 2, 1).astype(jnp.float32)
    acc = with_layout_constraint(acc.astype(jnp.bfloat16), Layout(major_to_minor=(0, 1)))
    return acc.T


def per_device(gate_pre, up_pre, grad_out, codes, scales):
    weight = decode(codes, scales)
    gate_value = gate_pre.astype(jnp.float32)
    up_value = up_pre.astype(jnp.float32)
    sigmoid_gate = jax.nn.sigmoid(gate_value)
    hidden = (gate_value * sigmoid_gate * up_value).astype(jnp.bfloat16)
    partial_out = jnp.dot(hidden, weight, preferred_element_type=jnp.float32).astype(jnp.bfloat16)
    out = lax.psum_scatter(partial_out, "tz", scatter_dimension=0, tiled=True)
    rows = out.shape[0] // 2
    ty = lax.axis_index("ty")
    out = lax.dynamic_slice_in_dim(out, ty * rows, rows, 0).astype(jnp.float32) + exchange(
        lax.dynamic_slice_in_dim(out, (1 - ty) * rows, rows, 0), "ty", 2, 1
    ).astype(jnp.float32)
    out = out.astype(jnp.bfloat16)
    cotangent = lax.all_gather(grad_out, "ty", axis=0, tiled=True)
    cotangent = lax.all_gather(cotangent, "tz", axis=0, tiled=True)
    grad_hidden = lax.dot_general(
        cotangent, weight, (((1,), (1,)), ((), ())), preferred_element_type=jnp.float32
    )
    grad_weight = weight_gradient(hidden, cotangent)
    grad_gate = (
        grad_hidden * up_value * sigmoid_gate * (1.0 + gate_value * (1.0 - sigmoid_gate))
    ).astype(jnp.bfloat16)
    grad_up = (grad_hidden * gate_value * sigmoid_gate).astype(jnp.bfloat16)
    return (out, grad_gate, grad_up, grad_weight)


def split_mesh(mesh):
    n_dp, n_tensor = mesh.shape["dp"], mesh.shape["tensor"]
    devices = mesh.devices.reshape(2, n_dp // 4, 2, n_tensor // 2, 2)
    return Mesh(devices, DP + TP)


def solution(mesh):
    fine = split_mesh(mesh)
    in_specs = (
        P(DP, TP),
        P(DP, TP),
        P(DP + TP, None),
        P(TP, None),
        P(TP, None),
    )
    out_specs = (P(DP + TP, None), P(DP, TP), P(DP, TP), P(TP, DP))
    return jax.shard_map(
        per_device, mesh=fine, in_specs=in_specs, out_specs=out_specs, check_vma=False
    )
```

```python
import jax
import jax.numpy as jnp
from jax import lax
from jax.experimental.layout import Layout, with_layout_constraint
from jax.sharding import Mesh, PartitionSpec as P

DP = ("dy", "dx", "dc")
TP = ("tz", "ty")


def decode(codes, scales):
    factor = jnp.exp2(scales.astype(jnp.float32) - 127.0).astype(jnp.bfloat16)
    blocks = codes.reshape(scales.shape[0], 32, codes.shape[1]) * factor[:, None, :]
    return blocks.reshape(codes.shape)


def exchange(value, axis, size, shift):
    perm = [(i, (i + shift) % size) for i in range(size)]
    return lax.ppermute(value, axis, perm)


def weight_gradient(hidden, cotangent):
    n_x = cotangent.shape[1] // 1024
    width = 256
    partial = lax.dot_general(
        cotangent, hidden, (((0,), (0,)), ((), ())), preferred_element_type=jnp.float32
    ).astype(jnp.bfloat16)
    partial = with_layout_constraint(partial, Layout(major_to_minor=(0, 1)))
    parts = partial.reshape(2, n_x, 2, width, partial.shape[1])
    dc = lax.axis_index("dc")
    mine = jnp.take(parts, dc, axis=2)
    arrived = exchange(jnp.take(parts, 1 - dc, axis=2), "dc", 2, 1)
    total = mine.astype(jnp.float32) + arrived.astype(jnp.float32)
    total = with_layout_constraint(total, Layout(major_to_minor=(0, 1, 2, 3)))
    group = ("dy", "dx")
    n = total.shape[0] * total.shape[1]
    total = total.reshape(n, *total.shape[2:])
    sent = total.astype(jnp.bfloat16)
    me = lax.axis_index(group)
    acc = jnp.take(total, me, axis=0)
    for shift in range(1, n):
        block = jnp.take(sent, (me + shift) % n, axis=0)
        acc = acc + exchange(block, group, n, shift).astype(jnp.float32)
    acc = with_layout_constraint(acc.astype(jnp.bfloat16), Layout(major_to_minor=(0, 1)))
    return acc.T


def per_device(gate_pre, up_pre, grad_out, codes, scales):
    weight = decode(codes, scales)
    gate_value = gate_pre.astype(jnp.float32)
    up_value = up_pre.astype(jnp.float32)
    sigmoid_gate = jax.nn.sigmoid(gate_value)
    hidden = (gate_value * sigmoid_gate * up_value).astype(jnp.bfloat16)
    partial_out = jnp.dot(hidden, weight, preferred_element_type=jnp.float32).astype(jnp.bfloat16)
    out = lax.psum_scatter(partial_out, "tz", scatter_dimension=0, tiled=True)
    rows = out.shape[0] // 2
    ty = lax.axis_index("ty")
    out = lax.dynamic_slice_in_dim(out, ty * rows, rows, 0).astype(jnp.float32) + exchange(
        lax.dynamic_slice_in_dim(out, (1 - ty) * rows, rows, 0), "ty", 2, 1
    ).astype(jnp.float32)
    out = out.astype(jnp.bfloat16)
    other = exchange(grad_out, "ty", 2, 1)
    first = ty == 0
    cotangent = jnp.concatenate(
        [jnp.where(first, grad_out, other), jnp.where(first, other, grad_out)], axis=0
    )
    cotangent = lax.all_gather(cotangent, "tz", axis=0, tiled=True)
    grad_hidden = lax.dot_general(
        cotangent, weight, (((1,), (1,)), ((), ())), preferred_element_type=jnp.float32
    )
    grad_weight = weight_gradient(hidden, cotangent)
    grad_gate = (
        grad_hidden * up_value * sigmoid_gate * (1.0 + gate_value * (1.0 - sigmoid_gate))
    ).astype(jnp.bfloat16)
    grad_up = (grad_hidden * gate_value * sigmoid_gate).astype(jnp.bfloat16)
    return (out, grad_gate, grad_up, grad_weight)


def split_mesh(mesh):
    n_dp, n_tensor = mesh.shape["dp"], mesh.shape["tensor"]
    devices = mesh.devices.reshape(2, n_dp // 4, 2, n_tensor // 2, 2)
    return Mesh(devices, DP + TP)


def solution(mesh):
    fine = split_mesh(mesh)
    in_specs = (
        P(DP, TP),
        P(DP, TP),
        P(DP + TP, None),
        P(TP, None),
        P(TP, None),
    )
    out_specs = (P(DP + TP, None), P(DP, TP), P(DP, TP), P(TP, DP))
    return jax.shard_map(
        per_device, mesh=fine, in_specs=in_specs, out_specs=out_specs, check_vma=False
    )
```

```python
import jax
import jax.numpy as jnp
from jax import lax
from jax.experimental.layout import Layout, with_layout_constraint
from jax.sharding import Mesh, PartitionSpec as P

DP = ("dy", "dx", "dc")
TP = ("tz", "ty")


def decode(codes, scales):
    factor = jnp.exp2(scales.astype(jnp.float32) - 127.0).astype(jnp.bfloat16)
    blocks = codes.reshape(scales.shape[0], 32, codes.shape[1]) * factor[:, None, :]
    return blocks.reshape(codes.shape)


def exchange(value, axis, size, shift):
    perm = [(i, (i + shift) % size) for i in range(size)]
    return lax.ppermute(value, axis, perm)


def half_sum(hidden, cotangent):
    n_x = cotangent.shape[1] // 512
    width = 256
    partial = lax.dot_general(
        cotangent, hidden, (((0,), (0,)), ((), ())), preferred_element_type=jnp.float32
    ).astype(jnp.bfloat16)
    partial = with_layout_constraint(partial, Layout(major_to_minor=(0, 1)))
    parts = partial.reshape(n_x, 2, width, partial.shape[1])
    dc = lax.axis_index("dc")
    mine = jnp.take(parts, dc, axis=1)
    arrived = exchange(jnp.take(parts, 1 - dc, axis=1), "dc", 2, 1)
    total = mine.astype(jnp.float32) + arrived.astype(jnp.float32)
    total = with_layout_constraint(total, Layout(major_to_minor=(0, 1, 2)))
    sent = total.astype(jnp.bfloat16)
    dx = lax.axis_index("dx")
    acc = jnp.take(total, dx, axis=0)
    for shift in range(1, n_x):
        block = jnp.take(sent, (dx + shift) % n_x, axis=0)
        acc = acc + exchange(block, "dx", n_x, shift).astype(jnp.float32)
    return acc


def weight_gradient(hidden, halves):
    sums = [half_sum(hidden, cot) for cot in halves]
    to_lo = lax.ppermute(sums[0].astype(jnp.bfloat16), "dy", [(1, 0)]).astype(jnp.float32)
    to_hi = lax.ppermute(sums[1].astype(jnp.bfloat16), "dy", [(0, 1)]).astype(jnp.float32)
    acc = jnp.where(lax.axis_index("dy") == 0, sums[0] + to_lo, sums[1] + to_hi)
    acc = with_layout_constraint(acc.astype(jnp.bfloat16), Layout(major_to_minor=(0, 1)))
    return acc.T


def per_device(gate_pre, up_pre, grad_out, codes, scales):
    weight = decode(codes, scales)
    gate_value = gate_pre.astype(jnp.float32)
    up_value = up_pre.astype(jnp.float32)
    sigmoid_gate = jax.nn.sigmoid(gate_value)
    hidden = (gate_value * sigmoid_gate * up_value).astype(jnp.bfloat16)
    partial_out = jnp.dot(hidden, weight, preferred_element_type=jnp.float32).astype(jnp.bfloat16)
    out = lax.psum_scatter(partial_out, "tz", scatter_dimension=0, tiled=True)
    rows = out.shape[0] // 2
    ty = lax.axis_index("ty")
    out = lax.dynamic_slice_in_dim(out, ty * rows, rows, 0).astype(jnp.float32) + exchange(
        lax.dynamic_slice_in_dim(out, (1 - ty) * rows, rows, 0), "ty", 2, 1
    ).astype(jnp.float32)
    out = out.astype(jnp.bfloat16)
    local = lax.all_gather(grad_out, "ty", axis=0, tiled=True)
    half = local.shape[1] // 2
    halves = [
        lax.all_gather(local[:, h * half:(h + 1) * half], "tz", axis=0, tiled=True) for h in range(2)
    ]
    cotangent = jnp.concatenate(halves, axis=1)
    grad_hidden = lax.dot_general(
        cotangent, weight, (((1,), (1,)), ((), ())), preferred_element_type=jnp.float32
    )
    grad_weight = weight_gradient(hidden, halves)
    grad_gate = (
        grad_hidden * up_value * sigmoid_gate * (1.0 + gate_value * (1.0 - sigmoid_gate))
    ).astype(jnp.bfloat16)
    grad_up = (grad_hidden * gate_value * sigmoid_gate).astype(jnp.bfloat16)
    return (out, grad_gate, grad_up, grad_weight)


def split_mesh(mesh):
    n_dp, n_tensor = mesh.shape["dp"], mesh.shape["tensor"]
    devices = mesh.devices.reshape(2, n_dp // 4, 2, n_tensor // 2, 2)
    return Mesh(devices, DP + TP)


def solution(mesh):
    fine = split_mesh(mesh)
    in_specs = (
        P(DP, TP),
        P(DP, TP),
        P(DP + TP, None),
        P(TP, None),
        P(TP, None),
    )
    out_specs = (P(DP + TP, None), P(DP, TP), P(DP, TP), P(TP, DP))
    return jax.shard_map(
        per_device, mesh=fine, in_specs=in_specs, out_specs=out_specs, check_vma=False
    )
```

```python
import jax
import jax.numpy as jnp
from jax import lax
from jax.experimental.layout import Layout, with_layout_constraint
from jax.sharding import Mesh, PartitionSpec as P

DP = ("dy", "dx", "dc")
TP = ("tz", "ty")


def decode(codes, scales):
    factor = jnp.exp2(scales.astype(jnp.float32) - 127.0).astype(jnp.bfloat16)
    blocks = codes.reshape(scales.shape[0], 32, codes.shape[1]) * factor[:, None, :]
    return blocks.reshape(codes.shape)


def exchange(value, axis, size, shift):
    perm = [(i, (i + shift) % size) for i in range(size)]
    return lax.ppermute(value, axis, perm)


def weight_gradient(hidden, cotangent):
    n_x = cotangent.shape[1] // 1024
    width = 256
    partial = lax.dot_general(
        cotangent, hidden, (((0,), (0,)), ((), ())), preferred_element_type=jnp.float32
    ).astype(jnp.bfloat16)
    partial = with_layout_constraint(partial, Layout(major_to_minor=(0, 1)))
    parts = partial.reshape(2, n_x, 2, width, partial.shape[1])
    dc = lax.axis_index("dc")
    mine = jnp.take(parts, dc, axis=2)
    arrived = exchange(jnp.take(parts, 1 - dc, axis=2), "dc", 2, 1)
    total = mine.astype(jnp.float32) + arrived.astype(jnp.float32)
    total = with_layout_constraint(total, Layout(major_to_minor=(0, 1, 2, 3)))
    dx = lax.axis_index("dx")
    rows = width // 2
    halves = (total[:, :, :rows], total[:, :, rows:])
    running = [None, None]
    for step in range(n_x - 1):
        for way, sign in ((0, 1), (1, -1)):
            own = jnp.take(halves[way], (dx - sign * (step + 1)) % n_x, axis=1)
            running[way] = own if step == 0 else running[way] + own
            running[way] = exchange(
                running[way].astype(jnp.bfloat16), "dx", n_x, sign % n_x
            ).astype(jnp.float32)
    acc = jnp.concatenate(
        [jnp.take(halves[way], dx, axis=1) + running[way] for way in range(2)], axis=1
    )
    dy = lax.axis_index("dy")
    sent = acc.astype(jnp.bfloat16)
    acc = jnp.take(acc, dy, axis=0) + exchange(jnp.take(sent, 1 - dy, axis=0), "dy", 2, 1).astype(jnp.float32)
    acc = with_layout_constraint(acc.astype(jnp.bfloat16), Layout(major_to_minor=(0, 1)))
    return acc.T


def per_device(gate_pre, up_pre, grad_out, codes, scales):
    weight = decode(codes, scales)
    gate_value = gate_pre.astype(jnp.float32)
    up_value = up_pre.astype(jnp.float32)
    sigmoid_gate = jax.nn.sigmoid(gate_value)
    hidden = (gate_value * sigmoid_gate * up_value).astype(jnp.bfloat16)
    partial_out = jnp.dot(hidden, weight, preferred_element_type=jnp.float32).astype(jnp.bfloat16)
    out = lax.psum_scatter(partial_out, "tz", scatter_dimension=0, tiled=True)
    rows = out.shape[0] // 2
    ty = lax.axis_index("ty")
    out = lax.dynamic_slice_in_dim(out, ty * rows, rows, 0).astype(jnp.float32) + exchange(
        lax.dynamic_slice_in_dim(out, (1 - ty) * rows, rows, 0), "ty", 2, 1
    ).astype(jnp.float32)
    out = out.astype(jnp.bfloat16)
    cotangent = lax.all_gather(grad_out, "ty", axis=0, tiled=True)
    cotangent = lax.all_gather(cotangent, "tz", axis=0, tiled=True)
    grad_hidden = lax.dot_general(
        cotangent, weight, (((1,), (1,)), ((), ())), preferred_element_type=jnp.float32
    )
    grad_weight = weight_gradient(hidden, cotangent)
    grad_gate = (
        grad_hidden * up_value * sigmoid_gate * (1.0 + gate_value * (1.0 - sigmoid_gate))
    ).astype(jnp.bfloat16)
    grad_up = (grad_hidden * gate_value * sigmoid_gate).astype(jnp.bfloat16)
    return (out, grad_gate, grad_up, grad_weight)


def split_mesh(mesh):
    n_dp, n_tensor = mesh.shape["dp"], mesh.shape["tensor"]
    devices = mesh.devices.reshape(2, n_dp // 4, 2, n_tensor // 2, 2)
    return Mesh(devices, DP + TP)


def solution(mesh):
    fine = split_mesh(mesh)
    in_specs = (
        P(DP, TP),
        P(DP, TP),
        P(DP + TP, None),
        P(TP, None),
        P(TP, None),
    )
    out_specs = (P(DP + TP, None), P(DP, TP), P(DP, TP), P(TP, DP))
    return jax.shard_map(
        per_device, mesh=fine, in_specs=in_specs, out_specs=out_specs, check_vma=False
    )
```

```python
import jax
import jax.numpy as jnp
from jax import lax
from jax.experimental.layout import Layout, with_layout_constraint
from jax.sharding import Mesh, PartitionSpec as P

DP = ("dy", "dx", "dc")
TP = ("tz", "ty")


def decode(codes, scales):
    factor = jnp.exp2(scales.astype(jnp.float32) - 127.0).astype(jnp.bfloat16)
    blocks = codes.reshape(scales.shape[0], 32, codes.shape[1]) * factor[:, None, :]
    return blocks.reshape(codes.shape)


def exchange(value, axis, size, shift):
    perm = [(i, (i + shift) % size) for i in range(size)]
    return lax.ppermute(value, axis, perm)


def weight_gradient(hidden, cotangent):
    n_x = cotangent.shape[1] // 1024
    width = 256
    partial = lax.dot_general(
        cotangent, hidden, (((0,), (0,)), ((), ())), preferred_element_type=jnp.float32
    ).astype(jnp.bfloat16)
    partial = with_layout_constraint(partial, Layout(major_to_minor=(0, 1)))
    parts = partial.reshape(2, n_x, 2, width, partial.shape[1])
    dc = lax.axis_index("dc")
    mine = jnp.take(parts, dc, axis=2)
    arrived = exchange(jnp.take(parts, 1 - dc, axis=2), "dc", 2, 1)
    total = mine.astype(jnp.float32) + arrived.astype(jnp.float32)
    total = with_layout_constraint(total, Layout(major_to_minor=(0, 1, 2, 3)))
    sent = total.astype(jnp.bfloat16)
    dx = lax.axis_index("dx")
    acc = jnp.take(total, dx, axis=1)
    if n_x == 4:
        ahead = jnp.take(sent, (dx + 1) % n_x, axis=1)
        behind = jnp.take(sent, (dx + 3) % n_x, axis=1)
        across = jnp.take(sent, (dx + 2) % n_x, axis=1)
        rows = width // 2
        relay_up = exchange(across[:, :rows], "dx", n_x, 1)
        relay_down = exchange(across[:, rows:], "dx", n_x, n_x - 1)
        acc = acc + exchange(ahead, "dx", n_x, 1).astype(jnp.float32)
        acc = acc + exchange(behind, "dx", n_x, n_x - 1).astype(jnp.float32)
        far = jnp.concatenate(
            [exchange(relay_up, "dx", n_x, 1), exchange(relay_down, "dx", n_x, n_x - 1)], axis=1
        )
        acc = acc + far.astype(jnp.float32)
    else:
        for shift in range(1, n_x):
            block = jnp.take(sent, (dx + shift) % n_x, axis=1)
            acc = acc + exchange(block, "dx", n_x, shift).astype(jnp.float32)
    dy = lax.axis_index("dy")
    sent = acc.astype(jnp.bfloat16)
    acc = jnp.take(acc, dy, axis=0) + exchange(jnp.take(sent, 1 - dy, axis=0), "dy", 2, 1).astype(jnp.float32)
    acc = with_layout_constraint(acc.astype(jnp.bfloat16), Layout(major_to_minor=(0, 1)))
    return acc.T


def per_device(gate_pre, up_pre, grad_out, codes, scales):
    weight = decode(codes, scales)
    gate_value = gate_pre.astype(jnp.float32)
    up_value = up_pre.astype(jnp.float32)
    sigmoid_gate = jax.nn.sigmoid(gate_value)
    hidden = (gate_value * sigmoid_gate * up_value).astype(jnp.bfloat16)
    partial_out = jnp.dot(hidden, weight, preferred_element_type=jnp.float32).astype(jnp.bfloat16)
    out = lax.psum_scatter(partial_out, "tz", scatter_dimension=0, tiled=True)
    rows = out.shape[0] // 2
    ty = lax.axis_index("ty")
    out = lax.dynamic_slice_in_dim(out, ty * rows, rows, 0).astype(jnp.float32) + exchange(
        lax.dynamic_slice_in_dim(out, (1 - ty) * rows, rows, 0), "ty", 2, 1
    ).astype(jnp.float32)
    out = out.astype(jnp.bfloat16)
    cotangent = lax.all_gather(grad_out, "ty", axis=0, tiled=True)
    cotangent = lax.all_gather(cotangent, "tz", axis=0, tiled=True)
    grad_hidden = lax.dot_general(
        cotangent, weight, (((1,), (1,)), ((), ())), preferred_element_type=jnp.float32
    )
    grad_weight = weight_gradient(hidden, cotangent)
    grad_gate = (
        grad_hidden * up_value * sigmoid_gate * (1.0 + gate_value * (1.0 - sigmoid_gate))
    ).astype(jnp.bfloat16)
    grad_up = (grad_hidden * gate_value * sigmoid_gate).astype(jnp.bfloat16)
    return (out, grad_gate, grad_up, grad_weight)


def split_mesh(mesh):
    n_dp, n_tensor = mesh.shape["dp"], mesh.shape["tensor"]
    devices = mesh.devices.reshape(2, n_dp // 4, 2, n_tensor // 2, 2)
    return Mesh(devices, DP + TP)


def solution(mesh):
    fine = split_mesh(mesh)
    in_specs = (
        P(DP, TP),
        P(DP, TP),
        P(DP + TP, None),
        P(TP, None),
        P(TP, None),
    )
    out_specs = (P(DP + TP, None), P(DP, TP), P(DP, TP), P(TP, DP))
    return jax.shard_map(
        per_device, mesh=fine, in_specs=in_specs, out_specs=out_specs, check_vma=False
    )
```

```python
import jax
import jax.numpy as jnp
from jax import lax
from jax.experimental.layout import Layout, with_layout_constraint
from jax.sharding import Mesh, PartitionSpec as P

DP = ("dy", "dx", "dc")
TP = ("tz", "ty")


def decode(codes, scales):
    factor = jnp.exp2(scales.astype(jnp.float32) - 127.0).astype(jnp.bfloat16)
    blocks = codes.reshape(scales.shape[0], 32, codes.shape[1]) * factor[:, None, :]
    return blocks.reshape(codes.shape)


def exchange(value, axis, size, shift):
    perm = [(i, (i + shift) % size) for i in range(size)]
    return lax.ppermute(value, axis, perm)


def weight_gradient(hidden, cotangent):
    n_x = cotangent.shape[1] // 1024
    width = 256
    partial = lax.dot_general(
        cotangent, hidden, (((0,), (0,)), ((), ())), preferred_element_type=jnp.float32
    ).astype(jnp.bfloat16)
    partial = with_layout_constraint(partial, Layout(major_to_minor=(0, 1)))
    parts = partial.reshape(2, n_x, 2, width, partial.shape[1])
    dc = lax.axis_index("dc")
    mine = jnp.take(parts, dc, axis=2)
    arrived = exchange(jnp.take(parts, 1 - dc, axis=2), "dc", 2, 1)
    sent = (mine.astype(jnp.float32) + arrived.astype(jnp.float32)).astype(jnp.bfloat16)
    sent = with_layout_constraint(sent, Layout(major_to_minor=(0, 1, 2, 3)))
    dx = lax.axis_index("dx")
    acc = jnp.take(sent, dx, axis=1).astype(jnp.float32)
    for shift in range(1, n_x):
        block = jnp.take(sent, (dx + shift) % n_x, axis=1)
        acc = acc + exchange(block, "dx", n_x, shift).astype(jnp.float32)
    dy = lax.axis_index("dy")
    sent = acc.astype(jnp.bfloat16)
    acc = jnp.take(acc, dy, axis=0) + exchange(jnp.take(sent, 1 - dy, axis=0), "dy", 2, 1).astype(jnp.float32)
    acc = with_layout_constraint(acc.astype(jnp.bfloat16), Layout(major_to_minor=(0, 1)))
    return acc.T


def per_device(gate_pre, up_pre, grad_out, codes, scales):
    weight = decode(codes, scales)
    gate_value = gate_pre.astype(jnp.float32)
    up_value = up_pre.astype(jnp.float32)
    sigmoid_gate = jax.nn.sigmoid(gate_value)
    hidden = (gate_value * sigmoid_gate * up_value).astype(jnp.bfloat16)
    partial_out = jnp.dot(hidden, weight, preferred_element_type=jnp.float32).astype(jnp.bfloat16)
    out = lax.psum_scatter(partial_out, "tz", scatter_dimension=0, tiled=True)
    rows = out.shape[0] // 2
    ty = lax.axis_index("ty")
    out = lax.dynamic_slice_in_dim(out, ty * rows, rows, 0).astype(jnp.float32) + exchange(
        lax.dynamic_slice_in_dim(out, (1 - ty) * rows, rows, 0), "ty", 2, 1
    ).astype(jnp.float32)
    out = out.astype(jnp.bfloat16)
    cotangent = lax.all_gather(grad_out, "ty", axis=0, tiled=True)
    cotangent = lax.all_gather(cotangent, "tz", axis=0, tiled=True)
    grad_hidden = lax.dot_general(
        cotangent, weight, (((1,), (1,)), ((), ())), preferred_element_type=jnp.float32
    )
    grad_weight = weight_gradient(hidden, cotangent)
    grad_gate = (
        grad_hidden * up_value * sigmoid_gate * (1.0 + gate_value * (1.0 - sigmoid_gate))
    ).astype(jnp.bfloat16)
    grad_up = (grad_hidden * gate_value * sigmoid_gate).astype(jnp.bfloat16)
    return (out, grad_gate, grad_up, grad_weight)


def split_mesh(mesh):
    n_dp, n_tensor = mesh.shape["dp"], mesh.shape["tensor"]
    devices = mesh.devices.reshape(2, n_dp // 4, 2, n_tensor // 2, 2)
    return Mesh(devices, DP + TP)


def solution(mesh):
    fine = split_mesh(mesh)
    in_specs = (
        P(DP, TP),
        P(DP, TP),
        P(DP + TP, None),
        P(TP, None),
        P(TP, None),
    )
    out_specs = (P(DP + TP, None), P(DP, TP), P(DP, TP), P(TP, DP))
    return jax.shard_map(
        per_device, mesh=fine, in_specs=in_specs, out_specs=out_specs, check_vma=False
    )
```

```python
import jax
import jax.numpy as jnp
from jax import lax
from jax.experimental.layout import Layout, with_layout_constraint
from jax.sharding import Mesh, PartitionSpec as P

DP = ("dy", "dx", "dc")
TP = ("tz", "ty")


def decode(codes, scales):
    factor = jnp.exp2(scales.astype(jnp.float32) - 127.0).astype(jnp.bfloat16)
    blocks = codes.reshape(scales.shape[0], 32, codes.shape[1]) * factor[:, None, :]
    return blocks.reshape(codes.shape)


def exchange(value, axis, size, shift):
    perm = [(i, (i + shift) % size) for i in range(size)]
    return lax.ppermute(value, axis, perm)


def weight_gradient(hidden, cotangent):
    n_x = cotangent.shape[1] // 1024
    width = 256
    partial = lax.dot_general(
        cotangent, hidden, (((0,), (0,)), ((), ())), preferred_element_type=jnp.float32
    ).astype(jnp.bfloat16)
    partial = with_layout_constraint(partial, Layout(major_to_minor=(0, 1)))
    parts = partial.reshape(2, n_x, 2, width, partial.shape[1])
    dc = lax.axis_index("dc")
    mine = jnp.take(parts, dc, axis=2)
    arrived = exchange(jnp.take(parts, 1 - dc, axis=2), "dc", 2, 1)
    total = mine.astype(jnp.float32) + arrived.astype(jnp.float32)
    total = with_layout_constraint(total, Layout(major_to_minor=(0, 1, 2, 3)))
    dy = lax.axis_index("dy")
    sent = total.astype(jnp.bfloat16)
    total = jnp.take(total, dy, axis=0) + exchange(jnp.take(sent, 1 - dy, axis=0), "dy", 2, 1).astype(jnp.float32)
    sent = total.astype(jnp.bfloat16)
    dx = lax.axis_index("dx")
    acc = jnp.take(total, dx, axis=0)
    for shift in range(1, n_x):
        block = jnp.take(sent, (dx + shift) % n_x, axis=0)
        acc = acc + exchange(block, "dx", n_x, shift).astype(jnp.float32)
    acc = with_layout_constraint(acc.astype(jnp.bfloat16), Layout(major_to_minor=(0, 1)))
    return acc.T


def per_device(gate_pre, up_pre, grad_out, codes, scales):
    weight = decode(codes, scales)
    gate_value = gate_pre.astype(jnp.float32)
    up_value = up_pre.astype(jnp.float32)
    sigmoid_gate = jax.nn.sigmoid(gate_value)
    hidden = (gate_value * sigmoid_gate * up_value).astype(jnp.bfloat16)
    partial_out = jnp.dot(hidden, weight, preferred_element_type=jnp.float32).astype(jnp.bfloat16)
    out = lax.psum_scatter(partial_out, "tz", scatter_dimension=0, tiled=True)
    rows = out.shape[0] // 2
    ty = lax.axis_index("ty")
    out = lax.dynamic_slice_in_dim(out, ty * rows, rows, 0).astype(jnp.float32) + exchange(
        lax.dynamic_slice_in_dim(out, (1 - ty) * rows, rows, 0), "ty", 2, 1
    ).astype(jnp.float32)
    out = out.astype(jnp.bfloat16)
    cotangent = lax.all_gather(grad_out, "ty", axis=0, tiled=True)
    cotangent = lax.all_gather(cotangent, "tz", axis=0, tiled=True)
    grad_hidden = lax.dot_general(
        cotangent, weight, (((1,), (1,)), ((), ())), preferred_element_type=jnp.float32
    )
    grad_weight = weight_gradient(hidden, cotangent)
    grad_gate = (
        grad_hidden * up_value * sigmoid_gate * (1.0 + gate_value * (1.0 - sigmoid_gate))
    ).astype(jnp.bfloat16)
    grad_up = (grad_hidden * gate_value * sigmoid_gate).astype(jnp.bfloat16)
    return (out, grad_gate, grad_up, grad_weight)


def split_mesh(mesh):
    n_dp, n_tensor = mesh.shape["dp"], mesh.shape["tensor"]
    devices = mesh.devices.reshape(2, n_dp // 4, 2, n_tensor // 2, 2)
    return Mesh(devices, DP + TP)


def solution(mesh):
    fine = split_mesh(mesh)
    in_specs = (
        P(DP, TP),
        P(DP, TP),
        P(DP + TP, None),
        P(TP, None),
        P(TP, None),
    )
    out_specs = (P(DP + TP, None), P(DP, TP), P(DP, TP), P(TP, DP))
    return jax.shard_map(
        per_device, mesh=fine, in_specs=in_specs, out_specs=out_specs, check_vma=False
    )
```
